32 devices in a mesh: wide: 16 (over z, y, x), narrow: 2 (over core).
Axes of the slice: x: 2, y: 2, z: 4, core: 2. Of those that a mesh axis runs over, the one named last changes fastest.
Arguments:
- sample_t: float32 [512, 65536], P(('wide', 'narrow')), may hold values from -300 to 300
Outputs:
- basis: float32 [65536, 512], P(('wide', 'narrow'))
- factor_out: float32 [512, 512], replicated
The draws below stay inside these ranges and needn't reach their ends.
All inputs are finite; a program needn't handle non-finite values.
Results may differ from the reference program's by a relative error of at most 0.000084.
Values sent between devices are 32-bit elements; how exact they have to be, the bound alone decides.
No kernel may reach another device: no remote copies, remote signals or barrier semaphores. Data moves between devices by JAX's collectives and lax.ppermute only.
A program may use at most 64 MiB of HBM per device.

```python
import math
import jax
import jax.numpy as jnp
from jax import lax

K = 512
ROWS = 65536


def draw_sample_t(key, part):
    keys = jax.random.split(key, 5)
    column_scale = jnp.exp(jax.random.uniform(keys[0], (K, 1), jnp.float32, 0.0, math.log(10.0)))
    row_rough = jnp.exp(jax.random.uniform(keys[1], (1, ROWS), jnp.float32, 0.0, math.log(10.0)))
    ramp = 1.0 + 2.0 * jnp.arange(ROWS, dtype=jnp.float32).reshape(1, ROWS) / (ROWS - 1)
    shared_rows = jax.random.truncated_normal(keys[3], -4.0, 4.0, (1, ROWS), jnp.float32)
    shared_cols = jax.random.truncated_normal(keys[4], -4.0, 4.0, (K, 1), jnp.float32)
    noise = jax.random.truncated_normal(keys[2], -4.0, 4.0, (K, ROWS), jnp.float32)
    common = 0.25
    return 0.1 * column_scale * row_rough * ramp * (noise + common * shared_cols * shared_rows)


def setup_inputs(seed: int = 0) -> dict:
    streams_of = jax.random.split(jax.random.key(seed), 2)
    return {
        "sample_t": draw_sample_t(jax.random.fold_in(streams_of[1], 71), 0),
    }


def factor_pair(matrix):
    lower = lax.linalg.cholesky(matrix)
    identity = jnp.eye(matrix.shape[0], dtype=matrix.dtype)
    solved = lax.linalg.triangular_solve(lower, identity, left_side=True, lower=True)
    return (lower, solved)

def reference(sample_t):
    gram_total = jnp.dot(sample_t.astype(jnp.float32), sample_t.T.astype(jnp.float32), precision=lax.Precision.HIGHEST, preferred_element_type=jnp.float32)
    lower, lower_inv = factor_pair(gram_total)
    upper_factor = lower.T
    inverse = lower_inv.T
    product = lax.dot_general(sample_t.astype(jnp.float32), inverse.astype(jnp.float32), (((0,), (0,)), ((), ())), precision=lax.Precision.HIGHEST, preferred_element_type=jnp.float32)
    scale_root = math.sqrt(ROWS)
    return (product * scale_root, upper_factor / scale_root)
```

```python
import math

import jax
import jax.numpy as jnp
from jax import lax
from jax.sharding import PartitionSpec as P

AXES = ("wide", "narrow")


def factor_pair(matrix):
    lower = lax.linalg.cholesky(matrix)
    identity = jnp.eye(matrix.shape[0], dtype=matrix.dtype)
    solved = lax.linalg.triangular_solve(lower, identity, left_side=True, lower=True)
    return (lower, solved)


def _pair(count, bit):
    return [(i, i ^ bit) for i in range(count)]


def sum_by_halving(local, count):
    steps = count.bit_length() - 1
    assert 1 << steps == count and local.shape[0] % count == 0
    idx = lax.axis_index(AXES)
    buf = local
    for k in range(steps):
        half = buf.shape[0] // 2
        b = (idx >> k) & 1
        keep = lax.dynamic_slice_in_dim(buf, b * half, half, 0)
        send = lax.dynamic_slice_in_dim(buf, (1 - b) * half, half, 0)
        buf = keep + lax.ppermute(send, AXES, _pair(count, 1 << k))
    for k in reversed(range(steps)):
        b = (idx >> k) & 1
        recv = lax.ppermute(buf, AXES, _pair(count, 1 << k))
        lo = jnp.where(b == 0, buf, recv)
        hi = jnp.where(b == 0, recv, buf)
        buf = jnp.concatenate([lo, hi], 0)
    return buf


def per_device(sample_t):
    wide_count = lax.axis_size("wide")
    narrow_count = lax.axis_size("narrow")
    count = wide_count * narrow_count
    rows_t = lax.all_to_all(sample_t, AXES, split_axis=1, concat_axis=0, tiled=True)
    gram_local = jnp.dot(
        rows_t, rows_t.T, precision=lax.Precision.HIGHEST, preferred_element_type=jnp.float32
    )
    gram_total = sum_by_halving(gram_local, count)
    lower, lower_inv = factor_pair(gram_total)
    upper_factor = lower.T
    inverse = lower_inv.T
    total_rows = rows_t.shape[1] * count
    scale_root = math.sqrt(total_rows)
    product = lax.dot_general(
        rows_t,
        inverse,
        (((0,), (0,)), ((), ())),
        precision=lax.Precision.HIGHEST,
        preferred_element_type=jnp.float32,
    )
    return (product * scale_root, upper_factor / scale_root)


def solution(mesh):
    in_specs = (P(AXES, None),)
    out_specs = (P(AXES, None), P())
    return jax.shard_map(
        per_device, mesh=mesh, in_specs=in_specs, out_specs=out_specs, check_vma=False
    )
```

```python
import math

import jax
import jax.numpy as jnp
from jax import lax
from jax.sharding import PartitionSpec as P

AXES = ("wide", "narrow")


def _mm(a, b):
    return jnp.dot(a, b, precision=lax.Precision.HIGHEST, preferred_element_type=jnp.float32)


def _diag_pair(block):
    lower = lax.linalg.cholesky(block)
    identity = jnp.eye(block.shape[0], dtype=block.dtype)
    solved = lax.linalg.triangular_solve(lower, identity, left_side=True, lower=True)
    return lower, solved


def factor_pair(matrix, b=128):
    n = matrix.shape[0]
    nb = n // b
    trail = matrix
    l_blk = {}
    d_inv = []
    for k in range(nb):
        l_kk, i_kk = _diag_pair(trail[:b, :b])
        d_inv.append(i_kk)
        l_blk[k, k] = l_kk
        if k < nb - 1:
            panel = _mm(trail[b:, :b], i_kk.T)
            for i in range(k + 1, nb):
                l_blk[i, k] = panel[(i - k - 1) * b:(i - k) * b]
            trail = trail[b:, b:] - _mm(panel, panel.T)
    inv = {}
    for j in range(nb):
        inv[j, j] = d_inv[j]
        for i in range(j + 1, nb):
            acc = _mm(l_blk[i, j], inv[j, j])
            for m in range(j + 1, i):
                acc = acc + _mm(l_blk[i, m], inv[m, j])
            inv[i, j] = -_mm(d_inv[i], acc)
    zero = jnp.zeros((b, b), matrix.dtype)
    lower = jnp.concatenate(
        [jnp.concatenate([l_blk.get((i, j), zero) for j in range(nb)], 1) for i in range(nb)], 0)
    lower_inv = jnp.concatenate(
        [jnp.concatenate([inv.get((i, j), zero) for j in range(nb)], 1) for i in range(nb)], 0)
    return (lower, lower_inv)


def _pair(count, bit):
    return [(i, i ^ bit) for i in range(count)]


def sum_by_halving(local, count):
    steps = count.bit_length() - 1
    assert 1 << steps == count and local.shape[0] % count == 0
    idx = lax.axis_index(AXES)
    buf = local
    for k in range(steps):
        half = buf.shape[0] // 2
        b = (idx >> k) & 1
        keep = lax.dynamic_slice_in_dim(buf, b * half, half, 0)
        send = lax.dynamic_slice_in_dim(buf, (1 - b) * half, half, 0)
        buf = keep + lax.ppermute(send, AXES, _pair(count, 1 << k))
    for k in reversed(range(steps)):
        b = (idx >> k) & 1
        recv = lax.ppermute(buf, AXES, _pair(count, 1 << k))
        lo = jnp.where(b == 0, buf, recv)
        hi = jnp.where(b == 0, recv, buf)
        buf = jnp.concatenate([lo, hi], 0)
    return buf


def per_device(sample_t):
    wide_count = lax.axis_size("wide")
    narrow_count = lax.axis_size("narrow")
    count = wide_count * narrow_count
    rows_t = lax.all_to_all(sample_t, AXES, split_axis=1, concat_axis=0, tiled=True)
    gram_local = jnp.dot(
        rows_t, rows_t.T, precision=lax.Precision.HIGHEST, preferred_element_type=jnp.float32
    )
    gram_total = sum_by_halving(gram_local, count)
    lower, lower_inv = factor_pair(gram_total)
    upper_factor = lower.T
    inverse = lower_inv.T
    total_rows = rows_t.shape[1] * count
    scale_root = math.sqrt(total_rows)
    product = lax.dot_general(
        rows_t,
        inverse,
        (((0,), (0,)), ((), ())),
        precision=lax.Precision.HIGHEST,
        preferred_element_type=jnp.float32,
    )
    return (product * scale_root, upper_factor / scale_root)


def solution(mesh):
    in_specs = (P(AXES, None),)
    out_specs = (P(AXES, None), P())
    return jax.shard_map(
        per_device, mesh=mesh, in_specs=in_specs, out_specs=out_specs, check_vma=False
    )
```

```python
import math

import jax
import jax.numpy as jnp
from jax import lax
from jax.experimental import pallas as pl
from jax.experimental.pallas import tpu as pltpu
from jax.sharding import PartitionSpec as P

AXES = ("wide", "narrow")


def _mm(a, b):
    return jnp.dot(a, b, precision=lax.Precision.HIGHEST, preferred_element_type=jnp.float32)


def _diag_kernel(a_ref, r_ref, w_ref, s_ref):
    b = a_ref.shape[0]
    s_ref[...] = a_ref[...]
    rows = lax.broadcasted_iota(jnp.int32, (b, 1), 0)
    lanes = lax.broadcasted_iota(jnp.int32, (1, b), 1)
    w_ref[...] = (lax.broadcasted_iota(jnp.int32, (b, b), 0)
                  == lax.broadcasted_iota(jnp.int32, (b, b), 1)).astype(jnp.float32)
    for j in range(b):
        lo = (j // 8) * 8
        a = s_ref[lo:, :]
        d = a[j - lo:j - lo + 1, j:j + 1]
        s = 1.0 / jnp.sqrt(d)
        row = jnp.where(lanes >= j, a[j - lo:j - lo + 1, :] * s, 0.0)
        col = jnp.where(rows[lo:] >= j, a[:, j:j + 1] * s, 0.0)
        r_ref[j:j + 1, :] = row
        s_ref[lo:, :] = a - col * row
        wrow = w_ref[j:j + 1, :] * s
        w_ref[j:j + 1, :] = wrow
        below = jnp.where(rows[lo:] > j, col, 0.0)
        w_ref[lo:, :] = w_ref[lo:, :] - below * wrow


def _diag_pair(block):
    b = block.shape[0]
    sym = (block + block.T) * 0.5
    r, w = pl.pallas_call(
        _diag_kernel,
        out_shape=(jax.ShapeDtypeStruct((b, b), jnp.float32),
                   jax.ShapeDtypeStruct((b, b), jnp.float32)),
        scratch_shapes=[pltpu.VMEM((b, b), jnp.float32)],
        cost_estimate=pl.CostEstimate(flops=4 * b * b * b, transcendentals=b,
                                      bytes_accessed=12 * b * b),
    )(sym)
    return r.T, w


def factor_pair(matrix, b=128):
    n = matrix.shape[0]
    nb = n // b
    trail = matrix
    l_blk = {}
    d_inv = []
    for k in range(nb):
        l_kk, i_kk = _diag_pair(trail[:b, :b])
        d_inv.append(i_kk)
        l_blk[k, k] = l_kk
        if k < nb - 1:
            panel = _mm(trail[b:, :b], i_kk.T)
            for i in range(k + 1, nb):
                l_blk[i, k] = panel[(i - k - 1) * b:(i - k) * b]
            trail = trail[b:, b:] - _mm(panel, panel.T)
    inv = {}
    for j in range(nb):
        inv[j, j] = d_inv[j]
        for i in range(j + 1, nb):
            acc = _mm(l_blk[i, j], inv[j, j])
            for m in range(j + 1, i):
                acc = acc + _mm(l_blk[i, m], inv[m, j])
            inv[i, j] = -_mm(d_inv[i], acc)
    zero = jnp.zeros((b, b), matrix.dtype)
    lower = jnp.concatenate(
        [jnp.concatenate([l_blk.get((i, j), zero) for j in range(nb)], 1) for i in range(nb)], 0)
    lower_inv = jnp.concatenate(
        [jnp.concatenate([inv.get((i, j), zero) for j in range(nb)], 1) for i in range(nb)], 0)
    return (lower, lower_inv)


def _pair(count, bit):
    return [(i, i ^ bit) for i in range(count)]


def sum_by_halving(local, count):
    steps = count.bit_length() - 1
    assert 1 << steps == count and local.shape[0] % count == 0
    idx = lax.axis_index(AXES)
    buf = local
    for k in range(steps):
        half = buf.shape[0] // 2
        b = (idx >> k) & 1
        keep = lax.dynamic_slice_in_dim(buf, b * half, half, 0)
        send = lax.dynamic_slice_in_dim(buf, (1 - b) * half, half, 0)
        buf = keep + lax.ppermute(send, AXES, _pair(count, 1 << k))
    for k in reversed(range(steps)):
        b = (idx >> k) & 1
        recv = lax.ppermute(buf, AXES, _pair(count, 1 << k))
        lo = jnp.where(b == 0, buf, recv)
        hi = jnp.where(b == 0, recv, buf)
        buf = jnp.concatenate([lo, hi], 0)
    return buf


def per_device(sample_t):
    wide_count = lax.axis_size("wide")
    narrow_count = lax.axis_size("narrow")
    count = wide_count * narrow_count
    rows_t = lax.all_to_all(sample_t, AXES, split_axis=1, concat_axis=0, tiled=True)
    gram_local = jnp.dot(
        rows_t, rows_t.T, precision=lax.Precision.HIGHEST, preferred_element_type=jnp.float32
    )
    gram_total = sum_by_halving(gram_local, count)
    lower, lower_inv = factor_pair(gram_total)
    upper_factor = lower.T
    inverse = lower_inv.T
    total_rows = rows_t.shape[1] * count
    scale_root = math.sqrt(total_rows)
    product = lax.dot_general(
        rows_t,
        inverse,
        (((0,), (0,)), ((), ())),
        precision=lax.Precision.HIGHEST,
        preferred_element_type=jnp.float32,
    )
    return (product * scale_root, upper_factor / scale_root)


def solution(mesh):
    in_specs = (P(AXES, None),)
    out_specs = (P(AXES, None), P())
    return jax.shard_map(
        per_device, mesh=mesh, in_specs=in_specs, out_specs=out_specs, check_vma=False
    )
```

```python
import math

import jax
import jax.numpy as jnp
from jax import lax
from jax.experimental import pallas as pl
from jax.sharding import PartitionSpec as P

AXES = ("wide", "narrow")


def _mm(a, b):
    return jnp.dot(a, b, precision=lax.Precision.HIGHEST, preferred_element_type=jnp.float32)


def _diag_kernel(a_ref, r_ref, w_ref):
    b = a_ref.shape[0]
    rows = lax.broadcasted_iota(jnp.int32, (b, 1), 0)
    lanes = lax.broadcasted_iota(jnp.int32, (1, b), 1)
    a = a_ref[...]
    w = (lax.broadcasted_iota(jnp.int32, (b, b), 0)
         == lax.broadcasted_iota(jnp.int32, (b, b), 1)).astype(jnp.float32)
    for j in range(b):
        s = lax.rsqrt(a[j:j + 1, j:j + 1])
        row = jnp.where(lanes >= j, a[j:j + 1, :] * s, 0.0)
        col = jnp.where(rows >= j, a[:, j:j + 1] * s, 0.0)
        r_ref[j:j + 1, :] = row
        a = a - col * row
        wrow = w[j:j + 1, :] * s
        below = jnp.where(rows > j, col, 0.0)
        w = w * jnp.where(rows == j, s, 1.0) - below * wrow
    w_ref[...] = w


def _diag_pair(block):
    b = block.shape[0]
    sym = (block + block.T) * 0.5
    r, w = pl.pallas_call(
        _diag_kernel,
        out_shape=(jax.ShapeDtypeStruct((b, b), jnp.float32),
                   jax.ShapeDtypeStruct((b, b), jnp.float32)),
        cost_estimate=pl.CostEstimate(flops=4 * b * b * b, transcendentals=b,
                                      bytes_accessed=12 * b * b),
    )(sym)
    return r.T, w


def factor_pair(matrix, b=128):
    n = matrix.shape[0]
    nb = n // b
    trail = matrix
    l_blk = {}
    d_inv = []
    for k in range(nb):
        l_kk, i_kk = _diag_pair(trail[:b, :b])
        d_inv.append(i_kk)
        l_blk[k, k] = l_kk
        if k < nb - 1:
            panel = _mm(trail[b:, :b], i_kk.T)
            for i in range(k + 1, nb):
                l_blk[i, k] = panel[(i - k - 1) * b:(i - k) * b]
            trail = trail[b:, b:] - _mm(panel, panel.T)
    inv = {}
    for j in range(nb):
        inv[j, j] = d_inv[j]
        for i in range(j + 1, nb):
            acc = _mm(l_blk[i, j], inv[j, j])
            for m in range(j + 1, i):
                acc = acc + _mm(l_blk[i, m], inv[m, j])
            inv[i, j] = -_mm(d_inv[i], acc)
    zero = jnp.zeros((b, b), matrix.dtype)
    lower = jnp.concatenate(
        [jnp.concatenate([l_blk.get((i, j), zero) for j in range(nb)], 1) for i in range(nb)], 0)
    lower_inv = jnp.concatenate(
        [jnp.concatenate([inv.get((i, j), zero) for j in range(nb)], 1) for i in range(nb)], 0)
    return (lower, lower_inv)


def _pair(count, bit):
    return [(i, i ^ bit) for i in range(count)]


def sum_by_halving(local, count):
    steps = count.bit_length() - 1
    assert 1 << steps == count and local.shape[0] % count == 0
    idx = lax.axis_index(AXES)
    buf = local
    for k in range(steps):
        half = buf.shape[0] // 2
        b = (idx >> k) & 1
        keep = lax.dynamic_slice_in_dim(buf, b * half, half, 0)
        send = lax.dynamic_slice_in_dim(buf, (1 - b) * half, half, 0)
        buf = keep + lax.ppermute(send, AXES, _pair(count, 1 << k))
    for k in reversed(range(steps)):
        b = (idx >> k) & 1
        recv = lax.ppermute(buf, AXES, _pair(count, 1 << k))
        lo = jnp.where(b == 0, buf, recv)
        hi = jnp.where(b == 0, recv, buf)
        buf = jnp.concatenate([lo, hi], 0)
    return buf


def per_device(sample_t):
    wide_count = lax.axis_size("wide")
    narrow_count = lax.axis_size("narrow")
    count = wide_count * narrow_count
    rows_t = lax.all_to_all(sample_t, AXES, split_axis=1, concat_axis=0, tiled=True)
    gram_local = jnp.dot(
        rows_t, rows_t.T, precision=lax.Precision.HIGHEST, preferred_element_type=jnp.float32
    )
    gram_total = sum_by_halving(gram_local, count)
    lower, lower_inv = factor_pair(gram_total)
    upper_factor = lower.T
    inverse = lower_inv.T
    total_rows = rows_t.shape[1] * count
    scale_root = math.sqrt(total_rows)
    product = lax.dot_general(
        rows_t,
        inverse,
        (((0,), (0,)), ((), ())),
        precision=lax.Precision.HIGHEST,
        preferred_element_type=jnp.float32,
    )
    return (product * scale_root, upper_factor / scale_root)


def solution(mesh):
    in_specs = (P(AXES, None),)
    out_specs = (P(AXES, None), P())
    return jax.shard_map(
        per_device, mesh=mesh, in_specs=in_specs, out_specs=out_specs, check_vma=False
    )
```

```python
import math

import jax
import jax.numpy as jnp
from jax import lax
from jax.experimental import pallas as pl
from jax.sharding import PartitionSpec as P

AXES = ("wide", "narrow")


def _mm(a, b):
    return jnp.dot(a, b, precision=lax.Precision.HIGHEST, preferred_element_type=jnp.float32)


def _diag_kernel(a_ref, r_ref, w_ref):
    b = a_ref.shape[0]
    rows = lax.broadcasted_iota(jnp.int32, (b, 1), 0)
    lanes = lax.broadcasted_iota(jnp.int32, (1, b), 1)
    a = a_ref[...]
    w = (lax.broadcasted_iota(jnp.int32, (b, b), 0)
         == lax.broadcasted_iota(jnp.int32, (b, b), 1)).astype(jnp.float32)
    for j in range(b):
        s = lax.rsqrt(a[j:j + 1, j:j + 1])
        row = jnp.where(lanes >= j, a[j:j + 1, :] * s, 0.0)
        col = jnp.where(rows >= j, a[:, j:j + 1] * s, 0.0)
        r_ref[j:j + 1, :] = row
        a = a - col * row
        wrow = w[j:j + 1, :] * s
        below = jnp.where(rows > j, col, 0.0)
        w = w * jnp.where(rows == j, s, 1.0) - below * wrow
    w_ref[...] = w


def _diag_pair(block):
    b = block.shape[0]
    sym = (block + block.T) * 0.5
    r, w = pl.pallas_call(
        _diag_kernel,
        out_shape=(jax.ShapeDtypeStruct((b, b), jnp.float32),
                   jax.ShapeDtypeStruct((b, b), jnp.float32)),
        cost_estimate=pl.CostEstimate(flops=4 * b * b * b, transcendentals=b,
                                      bytes_accessed=12 * b * b),
    )(sym)
    return r.T, w


def factor_pair(matrix, b=128):
    n = matrix.shape[0]
    nb = n // b
    trail = matrix
    l_blk = {}
    d_inv = []
    for k in range(nb):
        l_kk, i_kk = _diag_pair(trail[:b, :b])
        d_inv.append(i_kk)
        l_blk[k, k] = l_kk
        if k < nb - 1:
            panel = _mm(trail[b:, :b], i_kk.T)
            for i in range(k + 1, nb):
                l_blk[i, k] = panel[(i - k - 1) * b:(i - k) * b]
            trail = trail[b:, b:] - _mm(panel, panel.T)
    inv = {}
    for j in range(nb):
        inv[j, j] = d_inv[j]
        for i in range(j + 1, nb):
            acc = _mm(l_blk[i, j], inv[j, j])
            for m in range(j + 1, i):
                acc = acc + _mm(l_blk[i, m], inv[m, j])
            inv[i, j] = -_mm(d_inv[i], acc)
    zero = jnp.zeros((b, b), matrix.dtype)
    lower = jnp.concatenate(
        [jnp.concatenate([l_blk.get((i, j), zero) for j in range(nb)], 1) for i in range(nb)], 0)
    lower_inv = jnp.concatenate(
        [jnp.concatenate([inv.get((i, j), zero) for j in range(nb)], 1) for i in range(nb)], 0)
    return (lower, lower_inv)


def sum_by_radix(local, count):
    steps = count.bit_length() - 1
    assert 1 << steps == count and local.shape[0] % count == 0
    groups = [1] + [2] * ((steps - 1) // 2) + [1] * ((steps - 1) % 2)
    idx = lax.axis_index(AXES)
    buf = local
    plan = []
    k0 = 0
    for g in groups[:steps]:
        r = 1 << g
        t = (idx >> k0) & (r - 1)
        m = buf.shape[0] // r
        acc = lax.dynamic_slice_in_dim(buf, t * m, m, 0)
        for o in range(1, r):
            send = lax.dynamic_slice_in_dim(buf, (t ^ o) * m, m, 0)
            acc = acc + lax.ppermute(send, AXES, [(i, i ^ (o << k0)) for i in range(count)])
        buf = acc
        plan.append((k0, r, t))
        k0 += g
    for k0, r, t in reversed(plan):
        m = buf.shape[0]
        out = jnp.zeros((m * r,) + buf.shape[1:], buf.dtype)
        out = lax.dynamic_update_slice_in_dim(out, buf, t * m, 0)
        for o in range(1, r):
            recv = lax.ppermute(buf, AXES, [(i, i ^ (o << k0)) for i in range(count)])
            out = lax.dynamic_update_slice_in_dim(out, recv, (t ^ o) * m, 0)
        buf = out
    return buf


def per_device(sample_t):
    wide_count = lax.axis_size("wide")
    narrow_count = lax.axis_size("narrow")
    count = wide_count * narrow_count
    rows_t = lax.all_to_all(sample_t, AXES, split_axis=1, concat_axis=0, tiled=True)
    gram_local = jnp.dot(
        rows_t, rows_t.T, precision=lax.Precision.HIGHEST, preferred_element_type=jnp.float32
    )
    gram_total = sum_by_radix(gram_local, count)
    lower, lower_inv = factor_pair(gram_total)
    upper_factor = lower.T
    inverse = lower_inv.T
    total_rows = rows_t.shape[1] * count
    scale_root = math.sqrt(total_rows)
    product = lax.dot_general(
        rows_t,
        inverse,
        (((0,), (0,)), ((), ())),
        precision=lax.Precision.HIGHEST,
        preferred_element_type=jnp.float32,
    )
    return (product * scale_root, upper_factor / scale_root)


def solution(mesh):
    in_specs = (P(AXES, None),)
    out_specs = (P(AXES, None), P())
    return jax.shard_map(
        per_device, mesh=mesh, in_specs=in_specs, out_specs=out_specs, check_vma=False
    )
```

```python
import functools
import math

import jax
import jax.numpy as jnp
from jax import lax
from jax.experimental import pallas as pl
from jax.experimental.pallas import tpu as pltpu
from jax.sharding import PartitionSpec as P

AXES = ("wide", "narrow")


HI = lax.Precision.HIGHEST
NT = (((1,), (1,)), ((), ()))


def _nt(a, b):
    return lax.dot_general(a, b, NT, precision=HI, preferred_element_type=jnp.float32)


def _nn(a, b):
    return jnp.dot(a, b, precision=HI, preferred_element_type=jnp.float32)


def _chain(a, r_ref):
    b = a.shape[0]
    rows = lax.broadcasted_iota(jnp.int32, (b, 1), 0)
    lanes = lax.broadcasted_iota(jnp.int32, (1, b), 1)
    w = (lax.broadcasted_iota(jnp.int32, (b, b), 0)
         == lax.broadcasted_iota(jnp.int32, (b, b), 1)).astype(jnp.float32)
    for j in range(b):
        s = lax.rsqrt(a[j:j + 1, j:j + 1])
        row = jnp.where(lanes >= j, a[j:j + 1, :] * s, 0.0)
        col = jnp.where(rows >= j, a[:, j:j + 1] * s, 0.0)
        r_ref[j:j + 1, :] = row
        a = a - col * row
        wrow = w[j:j + 1, :] * s
        below = jnp.where(rows > j, col, 0.0)
        w = w * jnp.where(rows == j, s, 1.0) - below * wrow
    return w


def _factor_kernel(g_ref, l_ref, w_ref, t_ref, r_ref, *, b):
    n = g_ref.shape[0]
    nb = n // b
    t_ref[...] = g_ref[...]
    l_ref[...] = jnp.zeros_like(l_ref)
    w_ref[...] = jnp.zeros_like(w_ref)
    for k in range(nb):
        lo, hi = k * b, (k + 1) * b
        blk = t_ref[lo:hi, lo:hi]
        w_kk = _chain((blk + blk.T) * 0.5, r_ref)
        l_ref[lo:hi, lo:hi] = r_ref[...].T
        w_ref[lo:hi, lo:hi] = w_kk
        if k > 0:
            acc = _nn(l_ref[lo:hi, :lo], w_ref[:lo, :lo])
            w_ref[lo:hi, :lo] = -_nn(w_kk, acc)
        if k < nb - 1:
            panel = _nt(t_ref[hi:, lo:hi], w_kk)
            l_ref[hi:, lo:hi] = panel
            t_ref[hi:, hi:] = t_ref[hi:, hi:] - _nt(panel, panel)


def factor_pair(matrix, b=128):
    n = matrix.shape[0]
    return pl.pallas_call(
        functools.partial(_factor_kernel, b=b),
        out_shape=(jax.ShapeDtypeStruct((n, n), jnp.float32),
                   jax.ShapeDtypeStruct((n, n), jnp.float32)),
        scratch_shapes=[pltpu.VMEM((n, n), jnp.float32), pltpu.VMEM((b, b), jnp.float32)],
        cost_estimate=pl.CostEstimate(flops=2 * n * n * n, transcendentals=n,
                                      bytes_accessed=12 * n * n),
    )(matrix)


def _pair(count, bit):
    return [(i, i ^ bit) for i in range(count)]


def sum_by_halving(local, count):
    steps = count.bit_length() - 1
    assert 1 << steps == count and local.shape[0] % count == 0
    idx = lax.axis_index(AXES)
    buf = local
    for k in range(steps):
        half = buf.shape[0] // 2
        b = (idx >> k) & 1
        keep = lax.dynamic_slice_in_dim(buf, b * half, half, 0)
        send = lax.dynamic_slice_in_dim(buf, (1 - b) * half, half, 0)
        buf = keep + lax.ppermute(send, AXES, _pair(count, 1 << k))
    for k in reversed(range(steps)):
        b = (idx >> k) & 1
        recv = lax.ppermute(buf, AXES, _pair(count, 1 << k))
        lo = jnp.where(b == 0, buf, recv)
        hi = jnp.where(b == 0, recv, buf)
        buf = jnp.concatenate([lo, hi], 0)
    return buf


def per_device(sample_t):
    wide_count = lax.axis_size("wide")
    narrow_count = lax.axis_size("narrow")
    count = wide_count * narrow_count
    rows_t = lax.all_to_all(sample_t, AXES, split_axis=1, concat_axis=0, tiled=True)
    gram_local = jnp.dot(
        rows_t, rows_t.T, precision=lax.Precision.HIGHEST, preferred_element_type=jnp.float32
    )
    gram_total = sum_by_halving(gram_local, count)
    lower, lower_inv = factor_pair(gram_total)
    upper_factor = lower.T
    inverse = lower_inv.T
    total_rows = rows_t.shape[1] * count
    scale_root = math.sqrt(total_rows)
    product = lax.dot_general(
        rows_t,
        inverse,
        (((0,), (0,)), ((), ())),
        precision=lax.Precision.HIGHEST,
        preferred_element_type=jnp.float32,
    )
    return (product * scale_root, upper_factor / scale_root)


def solution(mesh):
    in_specs = (P(AXES, None),)
    out_specs = (P(AXES, None), P())
    return jax.shard_map(
        per_device, mesh=mesh, in_specs=in_specs, out_specs=out_specs, check_vma=False
    )
```

```python
import functools
import math

import jax
import jax.numpy as jnp
from jax import lax
from jax.experimental import pallas as pl
from jax.experimental.pallas import tpu as pltpu
from jax.sharding import PartitionSpec as P

AXES = ("wide", "narrow")


HI = lax.Precision.HIGHEST
NT = (((1,), (1,)), ((), ()))


def _nt(a, b):
    return lax.dot_general(a, b, NT, precision=HI, preferred_element_type=jnp.float32)


def _nn(a, b):
    return jnp.dot(a, b, precision=HI, preferred_element_type=jnp.float32)


def _chain(a, r_ref):
    b = a.shape[0]
    rows = lax.broadcasted_iota(jnp.int32, (b, 1), 0)
    lanes = lax.broadcasted_iota(jnp.int32, (1, b), 1)
    w = (lax.broadcasted_iota(jnp.int32, (b, b), 0)
         == lax.broadcasted_iota(jnp.int32, (b, b), 1)).astype(jnp.float32)
    for j in range(b):
        s = lax.rsqrt(a[j:j + 1, j:j + 1])
        row = jnp.where(lanes >= j, a[j:j + 1, :] * s, 0.0)
        col = jnp.where(rows >= j, a[:, j:j + 1] * s, 0.0)
        r_ref[j:j + 1, :] = row
        a = a - col * row
        wrow = w[j:j + 1, :] * s
        below = jnp.where(rows > j, col, 0.0)
        w = w * jnp.where(rows == j, s, 1.0) - below * wrow
    return w


def _factor_kernel(g_ref, l_ref, w_ref, t_ref, r_ref, *, b):
    n = g_ref.shape[0]
    nb = n // b
    t_ref[...] = g_ref[...]
    l_ref[...] = jnp.zeros_like(l_ref)
    w_ref[...] = jnp.zeros_like(w_ref)
    for k in range(nb):
        lo, hi = k * b, (k + 1) * b
        blk = t_ref[lo:hi, lo:hi]
        w_kk = _chain((blk + blk.T) * 0.5, r_ref)
        l_ref[lo:hi, lo:hi] = r_ref[...].T
        w_ref[lo:hi, lo:hi] = w_kk
        if k > 0:
            acc = _nn(l_ref[lo:hi, :lo], w_ref[:lo, :lo])
            w_ref[lo:hi, :lo] = -_nn(w_kk, acc)
        if k < nb - 1:
            panel = _nt(t_ref[hi:, lo:hi], w_kk)
            l_ref[hi:, lo:hi] = panel
            t_ref[hi:, hi:] = t_ref[hi:, hi:] - _nt(panel, panel)


def factor_pair(matrix, b=128):
    n = matrix.shape[0]
    return pl.pallas_call(
        functools.partial(_factor_kernel, b=b),
        out_shape=(jax.ShapeDtypeStruct((n, n), jnp.float32),
                   jax.ShapeDtypeStruct((n, n), jnp.float32)),
        scratch_shapes=[pltpu.VMEM((n, n), jnp.float32), pltpu.VMEM((b, b), jnp.float32)],
        cost_estimate=pl.CostEstimate(flops=2 * n * n * n, transcendentals=n,
                                      bytes_accessed=12 * n * n),
    )(matrix)


def _pair(count, bit):
    return [(i, i ^ bit) for i in range(count)]


def sum_by_halving(local, count):
    steps = count.bit_length() - 1
    assert 1 << steps == count and local.shape[0] % count == 0
    idx = lax.axis_index(AXES)
    buf = local
    for k in range(steps):
        half = buf.shape[0] // 2
        b = (idx >> k) & 1
        keep = lax.dynamic_slice_in_dim(buf, b * half, half, 0)
        send = lax.dynamic_slice_in_dim(buf, (1 - b) * half, half, 0)
        buf = keep + lax.ppermute(send, AXES, _pair(count, 1 << k))
    for k in reversed(range(steps)):
        b = (idx >> k) & 1
        recv = lax.ppermute(buf, AXES, _pair(count, 1 << k))
        lo = jnp.where(b == 0, buf, recv)
        hi = jnp.where(b == 0, recv, buf)
        buf = jnp.concatenate([lo, hi], 0)
    return buf


def per_device(sample_t):
    wide_count = lax.axis_size("wide")
    narrow_count = lax.axis_size("narrow")
    count = wide_count * narrow_count
    n_cols, n_all = sample_t.shape
    half = n_all // count // 2
    split = sample_t.reshape(n_cols, count, 2, half)
    parts = [
        lax.all_to_all(split[:, :, h, :].reshape(n_cols, count * half), AXES,
                       split_axis=1, concat_axis=0, tiled=True)
        for h in range(2)
    ]
    gram_local = None
    for part in parts:
        g = jnp.dot(part, part.T, precision=lax.Precision.HIGHEST,
                    preferred_element_type=jnp.float32)
        gram_local = g if gram_local is None else gram_local + g
    gram_total = sum_by_halving(gram_local, count)
    lower, lower_inv = factor_pair(gram_total)
    upper_factor = lower.T
    inverse = lower_inv.T
    total_rows = n_all
    scale_root = math.sqrt(total_rows)
    product = jnp.concatenate([
        lax.dot_general(
            part,
            inverse,
            (((0,), (0,)), ((), ())),
            precision=lax.Precision.HIGHEST,
            preferred_element_type=jnp.float32,
        )
        for part in parts
    ], 0)
    return (product * scale_root, upper_factor / scale_root)


def solution(mesh):
    in_specs = (P(AXES, None),)
    out_specs = (P(AXES, None), P())
    return jax.shard_map(
        per_device, mesh=mesh, in_specs=in_specs, out_specs=out_specs, check_vma=False
    )
```

```python
import functools
import math

import jax
import jax.numpy as jnp
from jax import lax
from jax.experimental import pallas as pl
from jax.experimental.pallas import tpu as pltpu
from jax.sharding import PartitionSpec as P

AXES = ("wide", "narrow")


HI = lax.Precision.HIGHEST
NT = (((1,), (1,)), ((), ()))


def _nt(a, b):
    return lax.dot_general(a, b, NT, precision=HI, preferred_element_type=jnp.float32)


def _nn(a, b):
    return jnp.dot(a, b, precision=HI, preferred_element_type=jnp.float32)


def _chain(a, r_ref):
    b = a.shape[0]
    rows = lax.broadcasted_iota(jnp.int32, (b, 1), 0)
    lanes = lax.broadcasted_iota(jnp.int32, (1, b), 1)
    w = (lax.broadcasted_iota(jnp.int32, (b, b), 0)
         == lax.broadcasted_iota(jnp.int32, (b, b), 1)).astype(jnp.float32)
    for j in range(b):
        s = lax.rsqrt(a[j:j + 1, j:j + 1])
        row = jnp.where(lanes >= j, a[j:j + 1, :] * s, 0.0)
        col = jnp.where(rows >= j, a[:, j:j + 1] * s, 0.0)
        r_ref[j:j + 1, :] = row
        a = a - col * row
        wrow = w[j:j + 1, :] * s
        below = jnp.where(rows > j, col, 0.0)
        w = w * jnp.where(rows == j, s, 1.0) - below * wrow
    return w


def _factor_kernel(g_ref, l_ref, w_ref, t_ref, r_ref, *, b):
    n = g_ref.shape[0]
    nb = n // b
    t_ref[...] = g_ref[...]
    l_ref[...] = jnp.zeros_like(l_ref)
    w_ref[...] = jnp.zeros_like(w_ref)
    for k in range(nb):
        lo, hi = k * b, (k + 1) * b
        blk = t_ref[lo:hi, lo:hi]
        w_kk = _chain((blk + blk.T) * 0.5, r_ref)
        l_ref[lo:hi, lo:hi] = r_ref[...].T
        w_ref[lo:hi, lo:hi] = w_kk
        if k > 0:
            acc = _nn(l_ref[lo:hi, :lo], w_ref[:lo, :lo])
            w_ref[lo:hi, :lo] = -_nn(w_kk, acc)
        if k < nb - 1:
            panel = _nt(t_ref[hi:, lo:hi], w_kk)
            l_ref[hi:, lo:hi] = panel
            t_ref[hi:, hi:] = t_ref[hi:, hi:] - _nt(panel, panel)


def factor_pair(matrix, b=128):
    n = matrix.shape[0]
    return pl.pallas_call(
        functools.partial(_factor_kernel, b=b),
        out_shape=(jax.ShapeDtypeStruct((n, n), jnp.float32),
                   jax.ShapeDtypeStruct((n, n), jnp.float32)),
        scratch_shapes=[pltpu.VMEM((n, n), jnp.float32), pltpu.VMEM((b, b), jnp.float32)],
        cost_estimate=pl.CostEstimate(flops=2 * n * n * n, transcendentals=n,
                                      bytes_accessed=12 * n * n),
    )(matrix)


def _basis_kernel(rt_ref, w_ref, o_ref, *, scale):
    y = _nn(w_ref[...], rt_ref[...])
    o_ref[...] = y.T * scale


def basis_rows(rows_t, lower_inv, scale, blk=256):
    k, m = rows_t.shape
    return pl.pallas_call(
        functools.partial(_basis_kernel, scale=scale),
        grid=(m // blk,),
        in_specs=[pl.BlockSpec((k, blk), lambda i: (0, i)),
                  pl.BlockSpec((k, k), lambda i: (0, 0))],
        out_specs=pl.BlockSpec((blk, k), lambda i: (i, 0)),
        out_shape=jax.ShapeDtypeStruct((m, k), jnp.float32),
        cost_estimate=pl.CostEstimate(flops=2 * m * k * k, transcendentals=0,
                                      bytes_accessed=4 * (2 * m * k + k * k)),
    )(rows_t, lower_inv)


def _pair(count, bit):
    return [(i, i ^ bit) for i in range(count)]


def sum_by_halving(local, count):
    steps = count.bit_length() - 1
    assert 1 << steps == count and local.shape[0] % count == 0
    idx = lax.axis_index(AXES)
    buf = local
    for k in range(steps):
        half = buf.shape[0] // 2
        b = (idx >> k) & 1
        keep = lax.dynamic_slice_in_dim(buf, b * half, half, 0)
        send = lax.dynamic_slice_in_dim(buf, (1 - b) * half, half, 0)
        buf = keep + lax.ppermute(send, AXES, _pair(count, 1 << k))
    for k in reversed(range(steps)):
        b = (idx >> k) & 1
        recv = lax.ppermute(buf, AXES, _pair(count, 1 << k))
        lo = jnp.where(b == 0, buf, recv)
        hi = jnp.where(b == 0, recv, buf)
        buf = jnp.concatenate([lo, hi], 0)
    return buf


def per_device(sample_t):
    wide_count = lax.axis_size("wide")
    narrow_count = lax.axis_size("narrow")
    count = wide_count * narrow_count
    rows_t = lax.all_to_all(sample_t, AXES, split_axis=1, concat_axis=0, tiled=True)
    gram_local = jnp.dot(
        rows_t, rows_t.T, precision=lax.Precision.HIGHEST, preferred_element_type=jnp.float32
    )
    gram_total = sum_by_halving(gram_local, count)
    lower, lower_inv = factor_pair(gram_total)
    upper_factor = lower.T
    total_rows = rows_t.shape[1] * count
    scale_root = math.sqrt(total_rows)
    product = basis_rows(rows_t, lower_inv, scale_root)
    return (product, upper_factor / scale_root)


def solution(mesh):
    in_specs = (P(AXES, None),)
    out_specs = (P(AXES, None), P())
    return jax.shard_map(
        per_device, mesh=mesh, in_specs=in_specs, out_specs=out_specs, check_vma=False
    )
```

```python
import functools
import math

import jax
import jax.numpy as jnp
from jax import lax
from jax.experimental import pallas as pl
from jax.experimental.pallas import tpu as pltpu
from jax.sharding import PartitionSpec as P

AXES = ("wide", "narrow")


HI = lax.Precision.HIGHEST
NT = (((1,), (1,)), ((), ()))


def _nt(a, b):
    return lax.dot_general(a, b, NT, precision=HI, preferred_element_type=jnp.float32)


def _nn(a, b):
    return jnp.dot(a, b, precision=HI, preferred_element_type=jnp.float32)


def _chain(a, r_ref):
    b = a.shape[0]
    rows = lax.broadcasted_iota(jnp.int32, (b, 1), 0)
    lanes = lax.broadcasted_iota(jnp.int32, (1, b), 1)
    w = (lax.broadcasted_iota(jnp.int32, (b, b), 0)
         == lax.broadcasted_iota(jnp.int32, (b, b), 1)).astype(jnp.float32)
    for j in range(b):
        s = lax.rsqrt(a[j:j + 1, j:j + 1])
        row = jnp.where(lanes >= j, a[j:j + 1, :] * s, 0.0)
        col = jnp.where(rows >= j, a[:, j:j + 1] * s, 0.0)
        r_ref[j:j + 1, :] = row
        a = a - col * row
        wrow = w[j:j + 1, :] * s
        below = jnp.where(rows > j, col, 0.0)
        w = w * jnp.where(rows == j, s, 1.0) - below * wrow
    return w


def _factor_kernel(g_ref, l_ref, w_ref, u_ref, t_ref, r_ref, *, b, scale):
    n = g_ref.shape[0]
    nb = n // b
    t_ref[...] = g_ref[...]
    l_ref[...] = jnp.zeros_like(l_ref)
    w_ref[...] = jnp.zeros_like(w_ref)
    for k in range(nb):
        lo, hi = k * b, (k + 1) * b
        blk = t_ref[lo:hi, lo:hi]
        w_kk = _chain((blk + blk.T) * 0.5, r_ref)
        l_ref[lo:hi, lo:hi] = r_ref[...].T
        w_ref[lo:hi, lo:hi] = w_kk
        if k > 0:
            acc = _nn(l_ref[lo:hi, :lo], w_ref[:lo, :lo])
            w_ref[lo:hi, :lo] = -_nn(w_kk, acc)
        if k < nb - 1:
            panel = _nt(t_ref[hi:, lo:hi], w_kk)
            l_ref[hi:, lo:hi] = panel
            t_ref[hi:, hi:] = t_ref[hi:, hi:] - _nt(panel, panel)
    u_ref[...] = l_ref[...].T / scale


def factor_pair(matrix, scale, b=128):
    n = matrix.shape[0]
    return pl.pallas_call(
        functools.partial(_factor_kernel, b=b, scale=scale),
        out_shape=(jax.ShapeDtypeStruct((n, n), jnp.float32),
                   jax.ShapeDtypeStruct((n, n), jnp.float32),
                   jax.ShapeDtypeStruct((n, n), jnp.float32)),
        scratch_shapes=[pltpu.VMEM((n, n), jnp.float32), pltpu.VMEM((b, b), jnp.float32)],
        cost_estimate=pl.CostEstimate(flops=2 * n * n * n, transcendentals=n,
                                      bytes_accessed=12 * n * n),
    )(matrix)


def _basis_kernel(rt_ref, w_ref, o_ref, *, scale):
    y = _nn(w_ref[...], rt_ref[...])
    o_ref[...] = y.T * scale


def basis_rows(rows_t, lower_inv, scale, blk=512):
    k, m = rows_t.shape
    return pl.pallas_call(
        functools.partial(_basis_kernel, scale=scale),
        grid=(m // blk,),
        in_specs=[pl.BlockSpec((k, blk), lambda i: (0, i)),
                  pl.BlockSpec((k, k), lambda i: (0, 0))],
        out_specs=pl.BlockSpec((blk, k), lambda i: (i, 0)),
        out_shape=jax.ShapeDtypeStruct((m, k), jnp.float32),
        cost_estimate=pl.CostEstimate(flops=2 * m * k * k, transcendentals=0,
                                      bytes_accessed=4 * (2 * m * k + k * k)),
    )(rows_t, lower_inv)


def _pair(count, bit):
    return [(i, i ^ bit) for i in range(count)]


def sum_by_halving(local, count):
    steps = count.bit_length() - 1
    assert 1 << steps == count and local.shape[0] % count == 0
    idx = lax.axis_index(AXES)
    buf = local
    for k in range(steps):
        half = buf.shape[0] // 2
        b = (idx >> k) & 1
        keep = lax.dynamic_slice_in_dim(buf, b * half, half, 0)
        send = lax.dynamic_slice_in_dim(buf, (1 - b) * half, half, 0)
        buf = keep + lax.ppermute(send, AXES, _pair(count, 1 << k))
    for k in reversed(range(steps)):
        b = (idx >> k) & 1
        recv = lax.ppermute(buf, AXES, _pair(count, 1 << k))
        lo = jnp.where(b == 0, buf, recv)
        hi = jnp.where(b == 0, recv, buf)
        buf = jnp.concatenate([lo, hi], 0)
    return buf


def per_device(sample_t):
    wide_count = lax.axis_size("wide")
    narrow_count = lax.axis_size("narrow")
    count = wide_count * narrow_count
    rows_t = lax.all_to_all(sample_t, AXES, split_axis=1, concat_axis=0, tiled=True)
    gram_local = jnp.dot(
        rows_t, rows_t.T, precision=lax.Precision.HIGHEST, preferred_element_type=jnp.float32
    )
    gram_total = sum_by_halving(gram_local, count)
    total_rows = rows_t.shape[1] * count
    scale_root = math.sqrt(total_rows)
    _, lower_inv, factor_out = factor_pair(gram_total, scale_root)
    product = basis_rows(rows_t, lower_inv, scale_root)
    return (product, factor_out)


def solution(mesh):
    in_specs = (P(AXES, None),)
    out_specs = (P(AXES, None), P())
    return jax.shard_map(
        per_device, mesh=mesh, in_specs=in_specs, out_specs=out_specs, check_vma=False
    )
```

```python
import functools
import math

import jax
import jax.numpy as jnp
from jax import lax
from jax.experimental import pallas as pl
from jax.experimental.pallas import tpu as pltpu
from jax.sharding import PartitionSpec as P

AXES = ("wide", "narrow")


HI = lax.Precision.HIGHEST
NT = (((1,), (1,)), ((), ()))


def _nt(a, b):
    return lax.dot_general(a, b, NT, precision=HI, preferred_element_type=jnp.float32)


def _nn(a, b):
    return jnp.dot(a, b, precision=HI, preferred_element_type=jnp.float32)


def _chain(a, r_ref):
    b = a.shape[0]
    rows = lax.broadcasted_iota(jnp.int32, (b, 1), 0)
    lanes = lax.broadcasted_iota(jnp.int32, (1, b), 1)
    w = (lax.broadcasted_iota(jnp.int32, (b, b), 0)
         == lax.broadcasted_iota(jnp.int32, (b, b), 1)).astype(jnp.float32)
    for j in range(b):
        s = lax.rsqrt(a[j:j + 1, j:j + 1])
        row = jnp.where(lanes >= j, a[j:j + 1, :] * s, 0.0)
        col = jnp.where(rows >= j, a[:, j:j + 1] * s, 0.0)
        r_ref[j:j + 1, :] = row
        a = a - col * row
        wrow = w[j:j + 1, :] * s
        below = jnp.where(rows > j, col, 0.0)
        w = w * jnp.where(rows == j, s, 1.0) - below * wrow
    return w


def _fused_kernel(g_ref, rt_ref, u_ref, o_ref, t_ref, r_ref, l_ref, w_ref, *, b, scale):
    n = g_ref.shape[0]
    nb = n // b
    t_ref[...] = g_ref[...]
    l_ref[...] = jnp.zeros_like(l_ref)
    w_ref[...] = jnp.zeros_like(w_ref)
    for k in range(nb):
        lo, hi = k * b, (k + 1) * b
        blk = t_ref[lo:hi, lo:hi]
        w_kk = _chain((blk + blk.T) * 0.5, r_ref)
        l_ref[lo:hi, lo:hi] = r_ref[...].T
        w_ref[lo:hi, lo:hi] = w_kk
        if k > 0:
            acc = _nn(l_ref[lo:hi, :lo], w_ref[:lo, :lo])
            w_ref[lo:hi, :lo] = -_nn(w_kk, acc)
        if k < nb - 1:
            panel = _nt(t_ref[hi:, lo:hi], w_kk)
            l_ref[hi:, lo:hi] = panel
            t_ref[hi:, hi:] = t_ref[hi:, hi:] - _nt(panel, panel)
        o_ref[:, lo:hi] = _nn(w_ref[lo:hi, :hi], rt_ref[:hi, :]).T * scale
    u_ref[...] = l_ref[...].T / scale


def factor_and_basis(gram, rows_t, scale, b=128):
    n = gram.shape[0]
    m = rows_t.shape[1]
    return pl.pallas_call(
        functools.partial(_fused_kernel, b=b, scale=scale),
        out_shape=(jax.ShapeDtypeStruct((n, n), jnp.float32),
                   jax.ShapeDtypeStruct((m, n), jnp.float32)),
        scratch_shapes=[pltpu.VMEM((n, n), jnp.float32), pltpu.VMEM((b, b), jnp.float32),
                        pltpu.VMEM((n, n), jnp.float32), pltpu.VMEM((n, n), jnp.float32)],
        cost_estimate=pl.CostEstimate(flops=2 * n * n * n + 2 * m * n * n, transcendentals=n,
                                      bytes_accessed=4 * (3 * n * n + 2 * m * n)),
    )(gram, rows_t)


def _pair(count, bit):
    return [(i, i ^ bit) for i in range(count)]


def sum_by_halving(local, count):
    steps = count.bit_length() - 1
    assert 1 << steps == count and local.shape[0] % count == 0
    idx = lax.axis_index(AXES)
    buf = local
    for k in range(steps):
        half = buf.shape[0] // 2
        b = (idx >> k) & 1
        keep = lax.dynamic_slice_in_dim(buf, b * half, half, 0)
        send = lax.dynamic_slice_in_dim(buf, (1 - b) * half, half, 0)
        buf = keep + lax.ppermute(send, AXES, _pair(count, 1 << k))
    for k in reversed(range(steps)):
        b = (idx >> k) & 1
        recv = lax.ppermute(buf, AXES, _pair(count, 1 << k))
        lo = jnp.where(b == 0, buf, recv)
        hi = jnp.where(b == 0, recv, buf)
        buf = jnp.concatenate([lo, hi], 0)
    return buf


def per_device(sample_t):
    wide_count = lax.axis_size("wide")
    narrow_count = lax.axis_size("narrow")
    count = wide_count * narrow_count
    rows_t = lax.all_to_all(sample_t, AXES, split_axis=1, concat_axis=0, tiled=True)
    gram_local = jnp.dot(
        rows_t, rows_t.T, precision=lax.Precision.HIGHEST, preferred_element_type=jnp.float32
    )
    gram_total = sum_by_halving(gram_local, count)
    total_rows = rows_t.shape[1] * count
    scale_root = math.sqrt(total_rows)
    factor_out, product = factor_and_basis(gram_total, rows_t, scale_root)
    return (product, factor_out)


def solution(mesh):
    in_specs = (P(AXES, None),)
    out_specs = (P(AXES, None), P())
    return jax.shard_map(
        per_device, mesh=mesh, in_specs=in_specs, out_specs=out_specs, check_vma=False
    )
```

```python
import functools
import math

import jax
import jax.numpy as jnp
from jax import lax
from jax.experimental import pallas as pl
from jax.experimental.pallas import tpu as pltpu
from jax.sharding import PartitionSpec as P

AXES = ("wide", "narrow")


HI = lax.Precision.HIGHEST
NT = (((1,), (1,)), ((), ()))


def _nt(a, b):
    return lax.dot_general(a, b, NT, precision=HI, preferred_element_type=jnp.float32)


def _nn(a, b):
    return jnp.dot(a, b, precision=HI, preferred_element_type=jnp.float32)


def _chain(a, r_ref, side=()):
    b = a.shape[0]
    rows = lax.broadcasted_iota(jnp.int32, (b, 1), 0)
    lanes = lax.broadcasted_iota(jnp.int32, (1, b), 1)
    w = (lax.broadcasted_iota(jnp.int32, (b, b), 0)
         == lax.broadcasted_iota(jnp.int32, (b, b), 1)).astype(jnp.float32)
    every = b // max(len(side), 1)
    for j in range(b):
        if side and j % every == 0 and j // every < len(side):
            side[j // every]()
        s = lax.rsqrt(a[j:j + 1, j:j + 1])
        row = jnp.where(lanes >= j, a[j:j + 1, :] * s, 0.0)
        col = jnp.where(rows >= j, a[:, j:j + 1] * s, 0.0)
        r_ref[j:j + 1, :] = row
        a = a - col * row
        wrow = w[j:j + 1, :] * s
        below = jnp.where(rows > j, col, 0.0)
        w = w * jnp.where(rows == j, s, 1.0) - below * wrow
    return w


def _fused_kernel(g_ref, rt_ref, u_ref, o_ref, t_ref, r_ref, l_ref, w_ref, *, b, scale):
    n = g_ref.shape[0]
    nb = n // b
    t_ref[...] = g_ref[...]
    l_ref[...] = jnp.zeros_like(l_ref)
    w_ref[...] = jnp.zeros_like(w_ref)
    m = rt_ref.shape[1]
    piece = m // 8

    def basis_piece(lo, hi, p):
        def run():
            cols = slice(p * piece, (p + 1) * piece)
            o_ref[cols, lo:hi] = _nn(w_ref[lo:hi, :hi], rt_ref[:hi, cols]).T * scale
        return run

    side = ()
    for k in range(nb):
        lo, hi = k * b, (k + 1) * b
        blk = t_ref[lo:hi, lo:hi]
        w_kk = _chain((blk + blk.T) * 0.5, r_ref, side)
        l_ref[lo:hi, lo:hi] = r_ref[...].T
        w_ref[lo:hi, lo:hi] = w_kk
        if k > 0:
            acc = _nn(l_ref[lo:hi, :lo], w_ref[:lo, :lo])
            w_ref[lo:hi, :lo] = -_nn(w_kk, acc)
        if k < nb - 1:
            panel = _nt(t_ref[hi:, lo:hi], w_kk)
            l_ref[hi:, lo:hi] = panel
            t_ref[hi:, hi:] = t_ref[hi:, hi:] - _nt(panel, panel)
        side = tuple(basis_piece(lo, hi, p) for p in range(8))
    for run in side:
        run()
    u_ref[...] = l_ref[...].T / scale


def factor_and_basis(gram, rows_t, scale, b=128):
    n = gram.shape[0]
    m = rows_t.shape[1]
    return pl.pallas_call(
        functools.partial(_fused_kernel, b=b, scale=scale),
        out_shape=(jax.ShapeDtypeStruct((n, n), jnp.float32),
                   jax.ShapeDtypeStruct((m, n), jnp.float32)),
        scratch_shapes=[pltpu.VMEM((n, n), jnp.float32), pltpu.VMEM((b, b), jnp.float32),
                        pltpu.VMEM((n, n), jnp.float32), pltpu.VMEM((n, n), jnp.float32)],
        cost_estimate=pl.CostEstimate(flops=2 * n * n * n + 2 * m * n * n, transcendentals=n,
                                      bytes_accessed=4 * (3 * n * n + 2 * m * n)),
    )(gram, rows_t)


def _pair(count, bit):
    return [(i, i ^ bit) for i in range(count)]


def sum_by_halving(local, count):
    steps = count.bit_length() - 1
    assert 1 << steps == count and local.shape[0] % count == 0
    idx = lax.axis_index(AXES)
    buf = local
    for k in range(steps):
        half = buf.shape[0] // 2
        b = (idx >> k) & 1
        keep = lax.dynamic_slice_in_dim(buf, b * half, half, 0)
        send = lax.dynamic_slice_in_dim(buf, (1 - b) * half, half, 0)
        buf = keep + lax.ppermute(send, AXES, _pair(count, 1 << k))
    for k in reversed(range(steps)):
        b = (idx >> k) & 1
        recv = lax.ppermute(buf, AXES, _pair(count, 1 << k))
        lo = jnp.where(b == 0, buf, recv)
        hi = jnp.where(b == 0, recv, buf)
        buf = jnp.concatenate([lo, hi], 0)
    return buf


def per_device(sample_t):
    wide_count = lax.axis_size("wide")
    narrow_count = lax.axis_size("narrow")
    count = wide_count * narrow_count
    rows_t = lax.all_to_all(sample_t, AXES, split_axis=1, concat_axis=0, tiled=True)
    gram_local = jnp.dot(
        rows_t, rows_t.T, precision=lax.Precision.HIGHEST, preferred_element_type=jnp.float32
    )
    gram_total = sum_by_halving(gram_local, count)
    total_rows = rows_t.shape[1] * count
    scale_root = math.sqrt(total_rows)
    factor_out, product = factor_and_basis(gram_total, rows_t, scale_root)
    return (product, factor_out)


def solution(mesh):
    in_specs = (P(AXES, None),)
    out_specs = (P(AXES, None), P())
    return jax.shard_map(
        per_device, mesh=mesh, in_specs=in_specs, out_specs=out_specs, check_vma=False
    )
```

```python
import functools
import math

import jax
import jax.numpy as jnp
from jax import lax
from jax.experimental import pallas as pl
from jax.experimental.pallas import tpu as pltpu
from jax.sharding import PartitionSpec as P

AXES = ("wide", "narrow")


HI = lax.Precision.HIGHEST
NT = (((1,), (1,)), ((), ()))


def _nt(a, b):
    return lax.dot_general(a, b, NT, precision=HI, preferred_element_type=jnp.float32)


def _nn(a, b):
    return jnp.dot(a, b, precision=HI, preferred_element_type=jnp.float32)


def _chain(a, r_ref, side=()):
    b = a.shape[0]
    rows = lax.broadcasted_iota(jnp.int32, (b, 1), 0)
    lanes = lax.broadcasted_iota(jnp.int32, (1, b), 1)
    w = (lax.broadcasted_iota(jnp.int32, (b, b), 0)
         == lax.broadcasted_iota(jnp.int32, (b, b), 1)).astype(jnp.float32)
    every = b // max(len(side), 1)
    for j in range(b):
        if side and j % every == 0 and j // every < len(side):
            side[j // every]()
        s = lax.rsqrt(a[j:j + 1, j:j + 1])
        row = jnp.where(lanes >= j, a[j:j + 1, :] * s, 0.0)
        col = jnp.where(rows >= j, a[:, j:j + 1] * s, 0.0)
        r_ref[j:j + 1, :] = row
        a = a - col * row
        wrow = w[j:j + 1, :] * s
        below = jnp.where(rows > j, col, 0.0)
        w = w * jnp.where(rows == j, s, 1.0) - below * wrow
    return w


def _fused_kernel(g_ref, rt_ref, u_ref, o_ref, t_ref, r_ref, l_ref, w_ref, *, b, scale):
    n = g_ref.shape[0]
    nb = n // b
    t_ref[...] = g_ref[...]
    l_ref[...] = jnp.zeros_like(l_ref)
    w_ref[...] = jnp.zeros_like(w_ref)
    m = rt_ref.shape[1]
    piece = m // 8

    def basis_piece(lo, hi, p):
        def run():
            cols = slice(p * piece, (p + 1) * piece)
            o_ref[cols, lo:hi] = _nn(w_ref[lo:hi, :hi], rt_ref[:hi, cols]).T * scale
        return run

    side = ()
    for k in range(nb):
        lo, hi = k * b, (k + 1) * b
        blk = t_ref[lo:hi, lo:hi]
        w_kk = _chain((blk + blk.T) * 0.5, r_ref, side)
        l_ref[lo:hi, lo:hi] = r_ref[...].T
        w_ref[lo:hi, lo:hi] = w_kk
        if k > 0:
            acc = _nn(l_ref[lo:hi, :lo], w_ref[:lo, :lo])
            w_ref[lo:hi, :lo] = -_nn(w_kk, acc)
        if k < nb - 1:
            panel = _nt(t_ref[hi:, lo:hi], w_kk)
            l_ref[hi:, lo:hi] = panel
            t_ref[hi:, hi:] = t_ref[hi:, hi:] - _nt(panel, panel)
        side = tuple(basis_piece(lo, hi, p) for p in range(8))
    for run in side:
        run()
    u_ref[...] = l_ref[...].T / scale


def factor_and_basis(gram, rows_t, scale, b=128):
    n = gram.shape[0]
    m = rows_t.shape[1]
    return pl.pallas_call(
        functools.partial(_fused_kernel, b=b, scale=scale),
        out_shape=(jax.ShapeDtypeStruct((n, n), jnp.float32),
                   jax.ShapeDtypeStruct((m, n), jnp.float32)),
        scratch_shapes=[pltpu.VMEM((n, n), jnp.float32), pltpu.VMEM((b, b), jnp.float32),
                        pltpu.VMEM((n, n), jnp.float32), pltpu.VMEM((n, n), jnp.float32)],
        cost_estimate=pl.CostEstimate(flops=2 * n * n * n + 2 * m * n * n, transcendentals=n,
                                      bytes_accessed=4 * (3 * n * n + 2 * m * n)),
    )(gram, rows_t)


def sum_by_halving(local, count):
    steps = count.bit_length() - 1
    assert 1 << steps == count and local.shape[0] % count == 0
    order = [list(range(steps)), list(range(steps))]
    if steps >= 3:
        order[1][1], order[1][2] = 2, 1
    idx = lax.axis_index(AXES)
    core = idx & 1
    buf = local
    rounds = []
    for r in range(steps):
        perm = [(i, i ^ (1 << order[i & 1][r])) for i in range(count)]
        bit = jnp.where(core == 0, order[0][r], order[1][r])
        rounds.append((perm, (idx >> bit) & 1))
    for perm, b in rounds:
        half = buf.shape[0] // 2
        keep = lax.dynamic_slice_in_dim(buf, b * half, half, 0)
        send = lax.dynamic_slice_in_dim(buf, (1 - b) * half, half, 0)
        buf = keep + lax.ppermute(send, AXES, perm)
    for perm, b in reversed(rounds):
        recv = lax.ppermute(buf, AXES, perm)
        lo = jnp.where(b == 0, buf, recv)
        hi = jnp.where(b == 0, recv, buf)
        buf = jnp.concatenate([lo, hi], 0)
    return buf


def per_device(sample_t):
    wide_count = lax.axis_size("wide")
    narrow_count = lax.axis_size("narrow")
    count = wide_count * narrow_count
    rows_t = lax.all_to_all(sample_t, AXES, split_axis=1, concat_axis=0, tiled=True)
    gram_local = jnp.dot(
        rows_t, rows_t.T, precision=lax.Precision.HIGHEST, preferred_element_type=jnp.float32
    )
    gram_total = sum_by_halving(gram_local, count)
    total_rows = rows_t.shape[1] * count
    scale_root = math.sqrt(total_rows)
    factor_out, product = factor_and_basis(gram_total, rows_t, scale_root)
    return (product, factor_out)


def solution(mesh):
    in_specs = (P(AXES, None),)
    out_specs = (P(AXES, None), P())
    return jax.shard_map(
        per_device, mesh=mesh, in_specs=in_specs, out_specs=out_specs, check_vma=False
    )
```

```python
import functools
import math

import jax
import jax.numpy as jnp
from jax import lax
from jax.experimental import pallas as pl
from jax.experimental.pallas import tpu as pltpu
from jax.sharding import PartitionSpec as P

AXES = ("wide", "narrow")


HI = lax.Precision.HIGHEST
NT = (((1,), (1,)), ((), ()))


def _nt(a, b):
    return lax.dot_general(a, b, NT, precision=HI, preferred_element_type=jnp.float32)


def _nn(a, b):
    return jnp.dot(a, b, precision=HI, preferred_element_type=jnp.float32)


def _chain(a, r_ref, side=()):
    b = a.shape[0]
    rows = lax.broadcasted_iota(jnp.int32, (b, 1), 0)
    lanes = lax.broadcasted_iota(jnp.int32, (1, b), 1)
    w = (lax.broadcasted_iota(jnp.int32, (b, b), 0)
         == lax.broadcasted_iota(jnp.int32, (b, b), 1)).astype(jnp.float32)
    every = b // max(len(side), 1)
    for j in range(b):
        if side and j % every == 0 and j // every < len(side):
            side[j // every]()
        s = lax.rsqrt(a[j:j + 1, j:j + 1])
        row = jnp.where(lanes >= j, a[j:j + 1, :] * s, 0.0)
        col = jnp.where(rows >= j, a[:, j:j + 1] * s, 0.0)
        r_ref[j:j + 1, :] = row
        a = a - col * row
        wrow = w[j:j + 1, :] * s
        below = jnp.where(rows > j, col, 0.0)
        w = w * jnp.where(rows == j, s, 1.0) - below * wrow
    return w


def _fused_kernel(g_ref, rt_ref, u_ref, o_ref, t_ref, r_ref, l_ref, w_ref, *, b, scale):
    n = g_ref.shape[0]
    nb = n // b
    t_ref[...] = g_ref[...]
    l_ref[...] = jnp.zeros_like(l_ref)
    w_ref[...] = jnp.zeros_like(w_ref)
    m = rt_ref.shape[1]
    piece = m // 8

    def basis_piece(lo, hi, p):
        def run():
            cols = slice(p * piece, (p + 1) * piece)
            o_ref[cols, lo:hi] = _nn(w_ref[lo:hi, :hi], rt_ref[:hi, cols]).T * scale
        return run

    side = ()
    for k in range(nb):
        lo, hi = k * b, (k + 1) * b
        blk = t_ref[lo:hi, lo:hi]
        w_kk = _chain((blk + blk.T) * 0.5, r_ref, side)
        l_ref[lo:hi, lo:hi] = r_ref[...].T
        w_ref[lo:hi, lo:hi] = w_kk
        if k > 0:
            acc = _nn(l_ref[lo:hi, :lo], w_ref[:lo, :lo])
            w_ref[lo:hi, :lo] = -_nn(w_kk, acc)
        if k < nb - 1:
            panel = _nt(t_ref[hi:, lo:hi], w_kk)
            l_ref[hi:, lo:hi] = panel
            t_ref[hi:, hi:] = t_ref[hi:, hi:] - _nt(panel, panel)
        side = tuple(basis_piece(lo, hi, p) for p in range(8))
    for run in side:
        run()
    u_ref[...] = l_ref[...].T / scale


def factor_and_basis(gram, rows_t, scale, b=128):
    n = gram.shape[0]
    m = rows_t.shape[1]
    return pl.pallas_call(
        functools.partial(_fused_kernel, b=b, scale=scale),
        out_shape=(jax.ShapeDtypeStruct((n, n), jnp.float32),
                   jax.ShapeDtypeStruct((m, n), jnp.float32)),
        scratch_shapes=[pltpu.VMEM((n, n), jnp.float32), pltpu.VMEM((b, b), jnp.float32),
                        pltpu.VMEM((n, n), jnp.float32), pltpu.VMEM((n, n), jnp.float32)],
        cost_estimate=pl.CostEstimate(flops=2 * n * n * n + 2 * m * n * n, transcendentals=n,
                                      bytes_accessed=4 * (3 * n * n + 2 * m * n)),
    )(gram, rows_t)


def sum_by_halving(local, count, first=None):
    steps = count.bit_length() - 1
    assert 1 << steps == count
    order = [list(range(steps)), list(range(steps))]
    if steps >= 3:
        order[1][1], order[1][2] = 2, 1
    idx = lax.axis_index(AXES)
    core = idx & 1
    buf = local
    rounds = []
    for r in range(steps):
        perm = [(i, i ^ (1 << order[i & 1][r])) for i in range(count)]
        bit = jnp.where(core == 0, order[0][r], order[1][r])
        rounds.append((perm, (idx >> bit) & 1))
    for r, (perm, b) in enumerate(rounds):
        if r == 0 and first is not None:
            send = first(1 - b)
            recv = lax.ppermute(send, AXES, perm)
            buf = first(b) + recv
            continue
        half = buf.shape[0] // 2
        keep = lax.dynamic_slice_in_dim(buf, b * half, half, 0)
        send = lax.dynamic_slice_in_dim(buf, (1 - b) * half, half, 0)
        buf = keep + lax.ppermute(send, AXES, perm)
    for perm, b in reversed(rounds):
        recv = lax.ppermute(buf, AXES, perm)
        lo = jnp.where(b == 0, buf, recv)
        hi = jnp.where(b == 0, recv, buf)
        buf = jnp.concatenate([lo, hi], 0)
    return buf


def per_device(sample_t):
    wide_count = lax.axis_size("wide")
    narrow_count = lax.axis_size("narrow")
    count = wide_count * narrow_count
    rows_t = lax.all_to_all(sample_t, AXES, split_axis=1, concat_axis=0, tiled=True)
    half = rows_t.shape[0] // 2

    def gram_half(h):
        part = lax.dynamic_slice_in_dim(rows_t, h * half, half, 0)
        return jnp.dot(part, rows_t.T, precision=lax.Precision.HIGHEST,
                       preferred_element_type=jnp.float32)

    gram_total = sum_by_halving(None, count, first=gram_half)
    total_rows = rows_t.shape[1] * count
    scale_root = math.sqrt(total_rows)
    factor_out, product = factor_and_basis(gram_total, rows_t, scale_root)
    return (product, factor_out)


def solution(mesh):
    in_specs = (P(AXES, None),)
    out_specs = (P(AXES, None), P())
    return jax.shard_map(
        per_device, mesh=mesh, in_specs=in_specs, out_specs=out_specs, check_vma=False
    )
```

```python
import functools
import math

import jax
import jax.numpy as jnp
from jax import lax
from jax.experimental import pallas as pl
from jax.experimental.pallas import tpu as pltpu
from jax.sharding import PartitionSpec as P

AXES = ("wide", "narrow")


HI = lax.Precision.HIGHEST
NT = (((1,), (1,)), ((), ()))


def _nt(a, b):
    return lax.dot_general(a, b, NT, precision=HI, preferred_element_type=jnp.float32)


def _nn(a, b):
    return jnp.dot(a, b, precision=HI, preferred_element_type=jnp.float32)


def _chain(a, r_ref, side=()):
    b = a.shape[0]
    rows = lax.broadcasted_iota(jnp.int32, (b, 1), 0)
    lanes = lax.broadcasted_iota(jnp.int32, (1, b), 1)
    w = (lax.broadcasted_iota(jnp.int32, (b, b), 0)
         == lax.broadcasted_iota(jnp.int32, (b, b), 1)).astype(jnp.float32)
    every = b // max(len(side), 1)
    for j in range(b):
        if side and j % every == 0 and j // every < len(side):
            side[j // every]()
        s = lax.rsqrt(a[j:j + 1, j:j + 1])
        row = jnp.where(lanes >= j, a[j:j + 1, :] * s, 0.0)
        col = jnp.where(rows >= j, a[:, j:j + 1] * s, 0.0)
        r_ref[j:j + 1, :] = row
        a = a - col * row
        wrow = w[j:j + 1, :] * s
        below = jnp.where(rows > j, col, 0.0)
        w = w * jnp.where(rows == j, s, 1.0) - below * wrow
    return w


def _fused_kernel(g_ref, rt_ref, u_ref, o_ref, t_ref, r_ref, l_ref, w_ref, *, b, scale):
    n = g_ref.shape[0]
    nb = n // b
    t_ref[...] = g_ref[...]
    l_ref[...] = jnp.zeros_like(l_ref)
    w_ref[...] = jnp.zeros_like(w_ref)
    m = rt_ref.shape[1]
    piece = m // 8

    def basis_piece(lo, hi, p):
        def run():
            cols = slice(p * piece, (p + 1) * piece)
            o_ref[cols, lo:hi] = _nn(w_ref[lo:hi, :hi], rt_ref[:hi, cols]).T * scale
        return run

    side = ()
    for k in range(nb):
        lo, hi = k * b, (k + 1) * b
        blk = t_ref[lo:hi, lo:hi]
        w_kk = _chain((blk + blk.T) * 0.5, r_ref, side)
        l_ref[lo:hi, lo:hi] = r_ref[...].T
        w_ref[lo:hi, lo:hi] = w_kk
        if k > 0:
            acc = _nn(l_ref[lo:hi, :lo], w_ref[:lo, :lo])
            w_ref[lo:hi, :lo] = -_nn(w_kk, acc)
        if k < nb - 1:
            panel = _nt(t_ref[hi:, lo:hi], w_kk)
            l_ref[hi:, lo:hi] = panel
            t_ref[hi:, hi:] = t_ref[hi:, hi:] - _nt(panel, panel)
        side = tuple(basis_piece(lo, hi, p) for p in range(8))
    for run in side:
        run()
    u_ref[...] = l_ref[...].T / scale


def factor_and_basis(gram, rows_t, scale, b=128):
    n = gram.shape[0]
    m = rows_t.shape[1]
    return pl.pallas_call(
        functools.partial(_fused_kernel, b=b, scale=scale),
        out_shape=(jax.ShapeDtypeStruct((n, n), jnp.float32),
                   jax.ShapeDtypeStruct((m, n), jnp.float32)),
        scratch_shapes=[pltpu.VMEM((n, n), jnp.float32), pltpu.VMEM((b, b), jnp.float32),
                        pltpu.VMEM((n, n), jnp.float32), pltpu.VMEM((n, n), jnp.float32)],
        cost_estimate=pl.CostEstimate(flops=2 * n * n * n + 2 * m * n * n, transcendentals=n,
                                      bytes_accessed=4 * (3 * n * n + 2 * m * n)),
    )(gram, rows_t)


def sum_by_halving(local, count):
    steps = count.bit_length() - 1
    assert 1 << steps == count and local.shape[0] % count == 0
    order = [list(range(steps)), list(range(steps))]
    if steps >= 3:
        order[1][1], order[1][2] = 2, 1
    idx = lax.axis_index(AXES)
    core = idx & 1
    buf = local
    rounds = []
    for r in range(steps):
        perm = [(i, i ^ (1 << order[i & 1][r])) for i in range(count)]
        bit = jnp.where(core == 0, order[0][r], order[1][r])
        rounds.append((perm, (idx >> bit) & 1))
    for perm, b in rounds:
        half = buf.shape[0] // 2
        keep = lax.dynamic_slice_in_dim(buf, b * half, half, 0)
        send = lax.dynamic_slice_in_dim(buf, (1 - b) * half, half, 0)
        buf = keep + lax.ppermute(send, AXES, perm)
    for perm, b in reversed(rounds):
        recv = lax.ppermute(buf, AXES, perm)
        lo = jnp.where(b == 0, buf, recv)
        hi = jnp.where(b == 0, recv, buf)
        buf = jnp.concatenate([lo, hi], 0)
    return buf


def per_device(sample_t):
    wide_count = lax.axis_size("wide")
    narrow_count = lax.axis_size("narrow")
    count = wide_count * narrow_count
    rows_t = lax.all_to_all(sample_t, AXES, split_axis=1, concat_axis=0, tiled=True)
    half = rows_t.shape[0] // 2
    top, bottom = rows_t[:half], rows_t[half:]

    def gram_of(x, y):
        return jnp.dot(x, y.T, precision=lax.Precision.HIGHEST,
                       preferred_element_type=jnp.float32)

    lower_left = gram_of(bottom, top)
    gram_local = jnp.concatenate([
        jnp.concatenate([gram_of(top, top), lower_left.T], 1),
        jnp.concatenate([lower_left, gram_of(bottom, bottom)], 1),
    ], 0)
    gram_total = sum_by_halving(gram_local, count)
    total_rows = rows_t.shape[1] * count
    scale_root = math.sqrt(total_rows)
    factor_out, product = factor_and_basis(gram_total, rows_t, scale_root)
    return (product, factor_out)


def solution(mesh):
    in_specs = (P(AXES, None),)
    out_specs = (P(AXES, None), P())
    return jax.shard_map(
        per_device, mesh=mesh, in_specs=in_specs, out_specs=out_specs, check_vma=False
    )
```

```python
import functools
import math

import jax
import jax.numpy as jnp
from jax import lax
from jax.experimental import pallas as pl
from jax.experimental.pallas import tpu as pltpu
from jax.sharding import PartitionSpec as P

AXES = ("wide", "narrow")


HI = lax.Precision.HIGHEST
NT = (((1,), (1,)), ((), ()))


def _nt(a, b):
    return lax.dot_general(a, b, NT, precision=HI, preferred_element_type=jnp.float32)


def _nn(a, b):
    return jnp.dot(a, b, precision=HI, preferred_element_type=jnp.float32)


def _chain(a, r_ref, side=()):
    b = a.shape[0]
    rows = lax.broadcasted_iota(jnp.int32, (b, 1), 0)
    lanes = lax.broadcasted_iota(jnp.int32, (1, b), 1)
    w = (lax.broadcasted_iota(jnp.int32, (b, b), 0)
         == lax.broadcasted_iota(jnp.int32, (b, b), 1)).astype(jnp.float32)
    every = b // max(len(side), 1)
    for j in range(b):
        if side and j % every == 0 and j // every < len(side):
            side[j // every]()
        s = lax.rsqrt(a[j:j + 1, j:j + 1])
        row = jnp.where(lanes >= j, a[j:j + 1, :] * s, 0.0)
        col = jnp.where(rows >= j, a[:, j:j + 1] * s, 0.0)
        r_ref[j:j + 1, :] = row
        a = a - col * row
        wrow = w[j:j + 1, :] * s
        below = jnp.where(rows > j, col, 0.0)
        w = w * jnp.where(rows == j, s, 1.0) - below * wrow
    return w


def _fused_kernel(g_ref, rt_ref, u_ref, o_ref, t_ref, r_ref, l_ref, w_ref, *, b, scale):
    n = g_ref.shape[0]
    nb = n // b
    t_ref[...] = g_ref[...]
    l_ref[...] = jnp.zeros_like(l_ref)
    w_ref[...] = jnp.zeros_like(w_ref)
    m = rt_ref.shape[1]
    piece = m // 8

    def basis_piece(lo, hi, p):
        def run():
            cols = slice(p * piece, (p + 1) * piece)
            o_ref[cols, lo:hi] = _nn(w_ref[lo:hi, :hi], rt_ref[:hi, cols]).T * scale
        return run

    side = ()
    for k in range(nb):
        lo, hi = k * b, (k + 1) * b
        blk = t_ref[lo:hi, lo:hi]
        w_kk = _chain((blk + blk.T) * 0.5, r_ref, side)
        l_ref[lo:hi, lo:hi] = r_ref[...].T
        w_ref[lo:hi, lo:hi] = w_kk
        if k > 0:
            acc = _nn(l_ref[lo:hi, :lo], w_ref[:lo, :lo])
            w_ref[lo:hi, :lo] = -_nn(w_kk, acc)
        if k < nb - 1:
            panel = _nt(t_ref[hi:, lo:hi], w_kk)
            l_ref[hi:, lo:hi] = panel
            t_ref[hi:, hi:] = t_ref[hi:, hi:] - _nt(panel, panel)
        side = tuple(basis_piece(lo, hi, p) for p in range(8))
    for run in side:
        run()
    u_ref[...] = l_ref[...].T / scale


def factor_and_basis(gram, rows_t, scale, b=128):
    n = gram.shape[0]
    m = rows_t.shape[1]
    return pl.pallas_call(
        functools.partial(_fused_kernel, b=b, scale=scale),
        out_shape=(jax.ShapeDtypeStruct((n, n), jnp.float32),
                   jax.ShapeDtypeStruct((m, n), jnp.float32)),
        scratch_shapes=[pltpu.VMEM((n, n), jnp.float32), pltpu.VMEM((b, b), jnp.float32),
                        pltpu.VMEM((n, n), jnp.float32), pltpu.VMEM((n, n), jnp.float32)],
        cost_estimate=pl.CostEstimate(flops=2 * n * n * n + 2 * m * n * n, transcendentals=n,
                                      bytes_accessed=4 * (3 * n * n + 2 * m * n)),
    )(gram, rows_t)


def sum_by_halving(local, count):
    steps = count.bit_length() - 1
    assert 1 << steps == count and local.shape[0] % count == 0
    order = [list(range(steps)), list(range(steps))]
    if steps >= 3:
        order[1][1], order[1][2] = 2, 1
    if steps >= 5:
        order[1][3], order[1][4] = 4, 3
    idx = lax.axis_index(AXES)
    core = idx & 1
    buf = local
    rounds = []
    for r in range(steps):
        perm = [(i, i ^ (1 << order[i & 1][r])) for i in range(count)]
        bit = jnp.where(core == 0, order[0][r], order[1][r])
        rounds.append((perm, (idx >> bit) & 1))
    for perm, b in rounds:
        half = buf.shape[0] // 2
        keep = lax.dynamic_slice_in_dim(buf, b * half, half, 0)
        send = lax.dynamic_slice_in_dim(buf, (1 - b) * half, half, 0)
        buf = keep + lax.ppermute(send, AXES, perm)
    for perm, b in reversed(rounds):
        recv = lax.ppermute(buf, AXES, perm)
        lo = jnp.where(b == 0, buf, recv)
        hi = jnp.where(b == 0, recv, buf)
        buf = jnp.concatenate([lo, hi], 0)
    return buf


def per_device(sample_t):
    wide_count = lax.axis_size("wide")
    narrow_count = lax.axis_size("narrow")
    count = wide_count * narrow_count
    rows_t = lax.all_to_all(sample_t, AXES, split_axis=1, concat_axis=0, tiled=True)
    half = rows_t.shape[0] // 2
    top, bottom = rows_t[:half], rows_t[half:]

    def gram_of(x, y):
        return jnp.dot(x, y.T, precision=lax.Precision.HIGHEST,
                       preferred_element_type=jnp.float32)

    lower_left = gram_of(bottom, top)
    gram_local = jnp.concatenate([
        jnp.concatenate([gram_of(top, top), lower_left.T], 1),
        jnp.concatenate([lower_left, gram_of(bottom, bottom)], 1),
    ], 0)
    gram_total = sum_by_halving(gram_local, count)
    total_rows = rows_t.shape[1] * count
    scale_root = math.sqrt(total_rows)
    factor_out, product = factor_and_basis(gram_total, rows_t, scale_root)
    return (product, factor_out)


def solution(mesh):
    in_specs = (P(AXES, None),)
    out_specs = (P(AXES, None), P())
    return jax.shard_map(
        per_device, mesh=mesh, in_specs=in_specs, out_specs=out_specs, check_vma=False
    )
```
